512 devices in a mesh: shot: 32 (over z_lo, y), recv: 16 (over z_hi, x, core).
Axes of the slice: x: 4, y: 8, z: 8 (z_hi: 2, z_lo: 4; z = z_hi * 4 + z_lo), core: 2. Of those that a mesh axis runs over, the one named last changes fastest.
Arguments:
- traces: bfloat16 [2, 2, 4096, 4096], P(None, None, 'shot', 'recv'), may hold values from -6 to 6
Outputs:
- multiples: float32 [2, 2, 4096, 4096], P(None, None, 'shot', 'recv')
The draws below stay inside these ranges and needn't reach their ends.
All inputs are finite; a program needn't handle non-finite values.
Results may differ from the reference program's by a relative error of at most 0.0044.
Values may be sent and summed in bfloat16 or wider, within the bound.
No kernel may reach another device: no remote copies, remote signals or barrier semaphores. Data moves between devices by JAX's collectives and lax.ppermute only.
A program may use at most 64 MiB of HBM per device.

```python
import jax
import jax.numpy as jnp
from jax import lax

NS = 4096
FREQ = 2


def steps_of(key, shape, cuts, low, high):
    gain = 1.0
    for dim, parts in cuts:
        steps = jax.random.uniform(jax.random.fold_in(jax.random.fold_in(key, 6), dim), (parts,), jnp.float32, low / len(cuts), high / len(cuts))
        gain = gain * jnp.repeat(jnp.exp(steps), shape[dim] // parts).reshape((-1,) + (1,) * (len(shape) - 1 - dim))
    return gain


def gaussian(key, shape, width, limit, split=(), held_as=jnp.bfloat16):
    result = jax.random.normal(key, shape, jnp.float32) * width
    if len(split) > 0:
        result = steps_of(key, shape, split, -0.22, 0.18) * result
    return jnp.clip(result, min=-limit, max=limit).astype(held_as)


def setup_inputs(seed: int = 0) -> dict:
    seeds = jax.random.split(jax.random.key(seed), 2)
    traces = gaussian(seeds[0], (FREQ, 2, NS, NS), 1.0, 6.0, ((2, 32), (3, 16)))
    return dict(traces=traces)


def mirror_average(component):
    summed = component.astype(jnp.float32) + jnp.transpose(component).astype(jnp.float32)
    return (summed * 0.5).astype(jnp.bfloat16)


def per_frequency(freq_data):
    real_avg = mirror_average(freq_data[0])
    imag_avg = mirror_average(freq_data[1])
    real_out = jnp.dot(real_avg, real_avg, preferred_element_type=jnp.float32) - jnp.dot(imag_avg, imag_avg, preferred_element_type=jnp.float32)
    imag_out = jnp.dot(real_avg, imag_avg, preferred_element_type=jnp.float32) + jnp.dot(imag_avg, real_avg, preferred_element_type=jnp.float32)
    scale_factor = jnp.float32(float(NS) ** -0.5)
    return jnp.stack((real_out, imag_out), axis=0) * scale_factor


def reference(traces):
    return lax.map(per_frequency, traces)
```

```python
import jax
import jax.numpy as jnp
from jax import lax
from jax.sharding import PartitionSpec as P

NS = 4096


def complex_product(left_block, right_block, form):
    real_real = jnp.einsum(
        form, left_block[:, 0], right_block[:, 0], preferred_element_type=jnp.float32
    )
    imag_imag = jnp.einsum(
        form, left_block[:, 1], right_block[:, 1], preferred_element_type=jnp.float32
    )
    real_imag = jnp.einsum(
        form, left_block[:, 0], right_block[:, 1], preferred_element_type=jnp.float32
    )
    imag_real = jnp.einsum(
        form, left_block[:, 1], right_block[:, 0], preferred_element_type=jnp.float32
    )
    return jnp.stack((real_real - imag_imag, real_imag + imag_real), axis=1)


def mirrored_pieces(traces, shot_count, recv_count):
    block_rows = traces.shape[2]
    g = traces.shape[3] // block_rows
    me_shot = lax.axis_index("shot")
    pieces = []
    for a in range(g):
        got = []
        for h in range(g):
            perm = [
                (s * recv_count + r, (g * r + h) * recv_count + s // g)
                for s in range(a, shot_count, g)
                for r in range(recv_count)
            ]
            part = traces[:, :, :, h * block_rows:(h + 1) * block_rows]
            got.append(lax.ppermute(part, ("shot", "recv"), perm))
        pieces.append(jnp.stack(got)[me_shot % g])
    return jnp.concatenate(pieces, axis=2)


def per_device(traces):
    recv_count = lax.axis_size("recv")
    shot_count = lax.axis_size("shot")
    mirrored = mirrored_pieces(traces, shot_count, recv_count)
    summed = traces.astype(jnp.float32) + jnp.swapaxes(mirrored, 2, 3).astype(jnp.float32)
    averaged = (summed * 0.5).astype(jnp.bfloat16)
    row_panel = lax.all_gather(averaged, "recv", axis=3, tiled=True)
    col_panel = lax.all_gather(averaged, "shot", axis=2, tiled=True)
    product = complex_product(row_panel, col_panel, "fik,fkj->fij")
    scale_factor = jnp.float32(float(NS) ** (-0.5))
    return product * scale_factor


def solution(mesh):
    placed = (P(None, None, "shot", "recv"),)
    return jax.shard_map(
        per_device,
        mesh=mesh,
        in_specs=placed,
        out_specs=P(None, None, "shot", "recv"),
        check_vma=False,
    )
```

```python
import jax
import jax.numpy as jnp
from jax import lax
from jax.sharding import PartitionSpec as P

NS = 4096


def complex_product(left_block, right_block, form):
    real_real = jnp.einsum(
        form, left_block[:, 0], right_block[:, 0], preferred_element_type=jnp.float32
    )
    imag_imag = jnp.einsum(
        form, left_block[:, 1], right_block[:, 1], preferred_element_type=jnp.float32
    )
    real_imag = jnp.einsum(
        form, left_block[:, 0], right_block[:, 1], preferred_element_type=jnp.float32
    )
    imag_real = jnp.einsum(
        form, left_block[:, 1], right_block[:, 0], preferred_element_type=jnp.float32
    )
    return jnp.stack((real_real - imag_imag, real_imag + imag_real), axis=1)


def stream_gather(block, axis, stride, n, wrap):
    axis_size = lax.axis_size(axis)
    pos = (lax.axis_index(axis) // stride) % n
    k_up = n // 2 if wrap else n - 1
    k_dn = n - 1 - k_up if wrap else n - 1

    def perm(step, direction):
        pairs = []
        for i in range(axis_size):
            p = (i // stride) % n
            q = (p + direction) % n if wrap else p + direction
            origin = p - direction * (step - 1)
            if not wrap and not (0 <= q < n and 0 <= origin < n):
                continue
            pairs.append((i, i + (q - p) * stride))
        return pairs

    ups, dns = [], []
    up = dn = block
    for k in range(1, max(k_up, k_dn) + 1):
        if k <= k_up:
            up = lax.ppermute(up, axis, perm(k, 1))
            ups.append(up)
        if k <= k_dn:
            dn = lax.ppermute(dn, axis, perm(k, -1))
            dns.append(dn)
    stacked = jnp.stack([block] + ups + dns)
    j = jnp.arange(n)
    if wrap:
        d = (pos - j) % n
        sel = jnp.where(d == 0, 0, jnp.where(d <= k_up, d, k_up + n - d))
    else:
        d = pos - j
        sel = jnp.where(d == 0, 0, jnp.where(d > 0, d, k_up - d))
    return jnp.take(stacked, sel, axis=0)


def mirrored_pieces(traces, shot_count, recv_count):
    block_rows = traces.shape[2]
    g = traces.shape[3] // block_rows
    me_shot = lax.axis_index("shot")
    pieces = []
    for a in range(g):
        got = []
        for h in range(g):
            perm = [
                (s * recv_count + r, (g * r + h) * recv_count + s // g)
                for s in range(a, shot_count, g)
                for r in range(recv_count)
            ]
            part = traces[:, :, :, h * block_rows:(h + 1) * block_rows]
            got.append(lax.ppermute(part, ("shot", "recv"), perm))
        pieces.append(jnp.stack(got)[me_shot % g])
    return jnp.concatenate(pieces, axis=2)


def per_device(traces):
    recv_count = lax.axis_size("recv")
    shot_count = lax.axis_size("shot")
    mirrored = mirrored_pieces(traces, shot_count, recv_count)
    summed = traces.astype(jnp.float32) + jnp.swapaxes(mirrored, 2, 3).astype(jnp.float32)
    averaged = (summed * 0.5).astype(jnp.bfloat16)
    freqs, _, block_rows, col_width = averaged.shape
    y_n, z_n = 8, shot_count // 8
    x_n, zh_n = 4, recv_count // 8
    first = stream_gather(averaged[:1], "shot", 1, y_n, True)
    first = stream_gather(first, "shot", y_n, z_n, False)
    second = stream_gather(averaged[1:], "shot", y_n, z_n, False)
    second = jnp.swapaxes(stream_gather(second, "shot", 1, y_n, True), 0, 1)
    cols = jnp.concatenate((first, second), axis=2)
    col_panel = jnp.transpose(cols, (2, 3, 0, 1, 4, 5)).reshape(freqs, 2, shot_count * block_rows, col_width)
    rows = stream_gather(averaged, "recv", 8, zh_n, True)
    rows = stream_gather(rows, "recv", 2, x_n, True)
    rows = stream_gather(rows, "recv", 1, 2, True)
    row_panel = jnp.transpose(rows, (3, 4, 5, 2, 1, 0, 6)).reshape(freqs, 2, block_rows, recv_count * col_width)
    product = complex_product(row_panel, col_panel, "fik,fkj->fij")
    scale_factor = jnp.float32(float(NS) ** (-0.5))
    return product * scale_factor


def solution(mesh):
    placed = (P(None, None, "shot", "recv"),)
    return jax.shard_map(
        per_device,
        mesh=mesh,
        in_specs=placed,
        out_specs=P(None, None, "shot", "recv"),
        check_vma=False,
    )
```

```python
import jax
import jax.numpy as jnp
from jax import lax
from jax.sharding import Mesh, PartitionSpec as P

NS = 4096
SHOT = ("z_lo", "y")
RECV = ("z_hi", "x", "core")


def complex_product(left_block, right_block, form):
    real_real = jnp.einsum(
        form, left_block[:, 0], right_block[:, 0], preferred_element_type=jnp.float32
    )
    imag_imag = jnp.einsum(
        form, left_block[:, 1], right_block[:, 1], preferred_element_type=jnp.float32
    )
    real_imag = jnp.einsum(
        form, left_block[:, 0], right_block[:, 1], preferred_element_type=jnp.float32
    )
    imag_real = jnp.einsum(
        form, left_block[:, 1], right_block[:, 0], preferred_element_type=jnp.float32
    )
    return jnp.stack((real_real - imag_imag, real_imag + imag_real), axis=1)


def stream_gather(block, axis, wrap):
    n = lax.axis_size(axis)
    axis_size, stride = n, 1
    pos = lax.axis_index(axis)
    k_up = n // 2 if wrap else n - 1
    k_dn = n - 1 - k_up if wrap else n - 1

    def perm(step, direction):
        pairs = []
        for i in range(axis_size):
            p = (i // stride) % n
            q = (p + direction) % n if wrap else p + direction
            origin = p - direction * (step - 1)
            if not wrap and not (0 <= q < n and 0 <= origin < n):
                continue
            pairs.append((i, i + (q - p) * stride))
        return pairs

    ups, dns = [], []
    up = dn = block
    for k in range(1, max(k_up, k_dn) + 1):
        if k <= k_up:
            up = lax.ppermute(up, axis, perm(k, 1))
            ups.append(up)
        if k <= k_dn:
            dn = lax.ppermute(dn, axis, perm(k, -1))
            dns.append(dn)
    stacked = jnp.stack([block] + ups + dns)
    j = jnp.arange(n)
    if wrap:
        d = (pos - j) % n
        sel = jnp.where(d == 0, 0, jnp.where(d <= k_up, d, k_up + n - d))
    else:
        d = pos - j
        sel = jnp.where(d == 0, 0, jnp.where(d > 0, d, k_up - d))
    return jnp.take(stacked, sel, axis=0)


def mirrored_pieces(traces, shot_count, recv_count):
    block_rows = traces.shape[2]
    g = traces.shape[3] // block_rows
    me_shot = lax.axis_index(SHOT)
    pieces = []
    for a in range(g):
        got = []
        for h in range(g):
            perm = [
                (s * recv_count + r, (g * r + h) * recv_count + s // g)
                for s in range(a, shot_count, g)
                for r in range(recv_count)
            ]
            part = traces[:, :, :, h * block_rows:(h + 1) * block_rows]
            got.append(lax.ppermute(part, SHOT + RECV, perm))
        pieces.append(jnp.stack(got)[me_shot % g])
    return jnp.concatenate(pieces, axis=2)


def per_device(traces):
    recv_count = lax.axis_size(RECV)
    shot_count = lax.axis_size(SHOT)
    mirrored = mirrored_pieces(traces, shot_count, recv_count)
    summed = traces.astype(jnp.float32) + jnp.swapaxes(mirrored, 2, 3).astype(jnp.float32)
    averaged = (summed * 0.5).astype(jnp.bfloat16)
    freqs, _, block_rows, col_width = averaged.shape
    first = stream_gather(stream_gather(averaged[:1], "y", True), "z_lo", False)
    second = jnp.swapaxes(stream_gather(stream_gather(averaged[1:], "z_lo", False), "y", True), 0, 1)
    cols = jnp.concatenate((first, second), axis=2)
    col_panel = jnp.transpose(cols, (2, 3, 0, 1, 4, 5)).reshape(freqs, 2, shot_count * block_rows, col_width)
    rows = lax.all_gather(averaged, "z_hi", axis=0)
    rows = lax.all_gather(rows, "x", axis=1)
    rows = lax.all_gather(rows, "core", axis=2)
    row_panel = jnp.transpose(rows, (3, 4, 5, 0, 1, 2, 6)).reshape(freqs, 2, block_rows, recv_count * col_width)
    product = complex_product(row_panel, col_panel, "fik,fkj->fij")
    scale_factor = jnp.float32(float(NS) ** (-0.5))
    return product * scale_factor


def solution(mesh):
    fine = Mesh(mesh.devices.reshape(4, 8, 2, 4, 2), SHOT + RECV)
    placed = P(None, None, SHOT, RECV)
    return jax.shard_map(
        per_device,
        mesh=fine,
        in_specs=(placed,),
        out_specs=placed,
        check_vma=False,
    )
```

```python
import jax
import jax.numpy as jnp
from jax import lax
from jax.sharding import Mesh, PartitionSpec as P

NS = 4096
SHOT = ("z_lo", "y")
RECV = ("z_hi", "x", "core")


def complex_product(left_block, right_block, form):
    real_real = jnp.einsum(
        form, left_block[:, 0], right_block[:, 0], preferred_element_type=jnp.float32
    )
    imag_imag = jnp.einsum(
        form, left_block[:, 1], right_block[:, 1], preferred_element_type=jnp.float32
    )
    real_imag = jnp.einsum(
        form, left_block[:, 0], right_block[:, 1], preferred_element_type=jnp.float32
    )
    imag_real = jnp.einsum(
        form, left_block[:, 1], right_block[:, 0], preferred_element_type=jnp.float32
    )
    return jnp.stack((real_real - imag_imag, real_imag + imag_real), axis=1)


def stream_gather(block, axis, wrap):
    n = lax.axis_size(axis)
    axis_size, stride = n, 1
    pos = lax.axis_index(axis)
    k_up = n // 2 if wrap else n - 1
    k_dn = n - 1 - k_up if wrap else n - 1

    def perm(step, direction):
        pairs = []
        for i in range(axis_size):
            p = (i // stride) % n
            q = (p + direction) % n if wrap else p + direction
            origin = p - direction * (step - 1)
            if not wrap and not (0 <= q < n and 0 <= origin < n):
                continue
            pairs.append((i, i + (q - p) * stride))
        return pairs

    ups, dns = [], []
    up = dn = block
    for k in range(1, max(k_up, k_dn) + 1):
        if k <= k_up:
            up = lax.ppermute(up, axis, perm(k, 1))
            ups.append(up)
        if k <= k_dn:
            dn = lax.ppermute(dn, axis, perm(k, -1))
            dns.append(dn)
    stacked = jnp.stack([block] + ups + dns)
    j = jnp.arange(n)
    if wrap:
        d = (pos - j) % n
        sel = jnp.where(d == 0, 0, jnp.where(d <= k_up, d, k_up + n - d))
    else:
        d = pos - j
        sel = jnp.where(d == 0, 0, jnp.where(d > 0, d, k_up - d))
    return jnp.take(stacked, sel, axis=0)


def mirrored_pieces(traces, shot_count, recv_count):
    block_rows = traces.shape[2]
    g = traces.shape[3] // block_rows
    me_shot = lax.axis_index(SHOT)
    pieces = []
    for a in range(g):
        got = []
        for h in range(g):
            perm = [
                (s * recv_count + r, (g * r + h) * recv_count + s // g)
                for s in range(a, shot_count, g)
                for r in range(recv_count)
            ]
            part = traces[:, :, :, h * block_rows:(h + 1) * block_rows]
            got.append(lax.ppermute(part, SHOT + RECV, perm))
        pieces.append(jnp.stack(got)[me_shot % g])
    return jnp.concatenate(pieces, axis=2)


def per_device(traces):
    recv_count = lax.axis_size(RECV)
    shot_count = lax.axis_size(SHOT)
    mirrored = mirrored_pieces(traces, shot_count, recv_count)
    summed = traces.astype(jnp.float32) + jnp.swapaxes(mirrored, 2, 3).astype(jnp.float32)
    averaged = (summed * 0.5).astype(jnp.bfloat16)
    freqs, _, block_rows, col_width = averaged.shape
    cols = stream_gather(stream_gather(averaged, "z_lo", False), "y", True)
    col_panel = jnp.transpose(cols, (2, 3, 1, 0, 4, 5)).reshape(freqs, 2, shot_count * block_rows, col_width)
    rows = stream_gather(averaged, "z_hi", True)
    rows = lax.all_gather(rows, "x", axis=1)
    rows = lax.all_gather(rows, "core", axis=2)
    row_panel = jnp.transpose(rows, (3, 4, 5, 0, 1, 2, 6)).reshape(freqs, 2, block_rows, recv_count * col_width)
    product = complex_product(row_panel, col_panel, "fik,fkj->fij")
    scale_factor = jnp.float32(float(NS) ** (-0.5))
    return product * scale_factor


def solution(mesh):
    fine = Mesh(mesh.devices.reshape(4, 8, 2, 4, 2), SHOT + RECV)
    placed = P(None, None, SHOT, RECV)
    return jax.shard_map(
        per_device,
        mesh=fine,
        in_specs=(placed,),
        out_specs=placed,
        check_vma=False,
    )
```

```python
import jax
import jax.numpy as jnp
from jax import lax
from jax.sharding import Mesh, PartitionSpec as P

NS = 4096
SHOT = ("z_lo", "y")
RECV = ("z_hi", "x", "core")


def complex_product(left_block, right_block, form):
    real_real = jnp.einsum(
        form, left_block[:, 0], right_block[:, 0], preferred_element_type=jnp.float32
    )
    imag_imag = jnp.einsum(
        form, left_block[:, 1], right_block[:, 1], preferred_element_type=jnp.float32
    )
    real_imag = jnp.einsum(
        form, left_block[:, 0], right_block[:, 1], preferred_element_type=jnp.float32
    )
    imag_real = jnp.einsum(
        form, left_block[:, 1], right_block[:, 0], preferred_element_type=jnp.float32
    )
    return jnp.stack((real_real - imag_imag, real_imag + imag_real), axis=1)


def stream_gather(block, axis, wrap):
    n = lax.axis_size(axis)
    axis_size, stride = n, 1
    pos = lax.axis_index(axis)
    k_up = n // 2 if wrap else n - 1
    k_dn = n - 1 - k_up if wrap else n - 1

    def perm(step, direction):
        pairs = []
        for i in range(axis_size):
            p = (i // stride) % n
            q = (p + direction) % n if wrap else p + direction
            origin = p - direction * (step - 1)
            if not wrap and not (0 <= q < n and 0 <= origin < n):
                continue
            pairs.append((i, i + (q - p) * stride))
        return pairs

    ups, dns = [], []
    up = dn = block
    for k in range(1, max(k_up, k_dn) + 1):
        if k <= k_up:
            up = lax.ppermute(up, axis, perm(k, 1))
            ups.append(up)
        if k <= k_dn:
            dn = lax.ppermute(dn, axis, perm(k, -1))
            dns.append(dn)
    stacked = jnp.stack([block] + ups + dns)
    j = jnp.arange(n)
    if wrap:
        d = (pos - j) % n
        sel = jnp.where(d == 0, 0, jnp.where(d <= k_up, d, k_up + n - d))
    else:
        d = pos - j
        sel = jnp.where(d == 0, 0, jnp.where(d > 0, d, k_up - d))
    return jnp.take(stacked, sel, axis=0)


def ring_blocks(block, axis):
    n = lax.axis_size(axis)
    right = [(i, (i + 1) % n) for i in range(n)]
    left = [(d, s) for s, d in right]
    got = [(0, block)]
    up = dn = block
    for k in range(1, n // 2 + 1):
        up = lax.ppermute(up, axis, right)
        got.append((k, up))
        if k < n - n // 2:
            dn = lax.ppermute(dn, axis, left)
            got.append((-k, dn))
    return got


def mirrored_pieces(traces, shot_count, recv_count):
    block_rows = traces.shape[2]
    g = traces.shape[3] // block_rows
    me_shot = lax.axis_index(SHOT)
    pieces = []
    for a in range(g):
        got = []
        for h in range(g):
            perm = [
                (s * recv_count + r, (g * r + h) * recv_count + s // g)
                for s in range(a, shot_count, g)
                for r in range(recv_count)
            ]
            part = traces[:, :, :, h * block_rows:(h + 1) * block_rows]
            got.append(lax.ppermute(part, SHOT + RECV, perm))
        pieces.append(jnp.stack(got)[me_shot % g])
    return jnp.concatenate(pieces, axis=2)


def per_device(traces):
    recv_count = lax.axis_size(RECV)
    shot_count = lax.axis_size(SHOT)
    mirrored = mirrored_pieces(traces, shot_count, recv_count)
    summed = traces.astype(jnp.float32) + jnp.swapaxes(mirrored, 2, 3).astype(jnp.float32)
    averaged = (summed * 0.5).astype(jnp.bfloat16)
    freqs, _, block_rows, col_width = averaged.shape
    z_cols = jnp.moveaxis(stream_gather(averaged, "z_lo", False), 0, 2)
    rows = stream_gather(averaged, "z_hi", True)
    rows = lax.all_gather(rows, "x", axis=1)
    rows = lax.all_gather(rows, "core", axis=2)
    y_n = lax.axis_size("y")
    z_n = z_cols.shape[2]
    row_panel = jnp.transpose(rows, (3, 4, 5, 0, 1, 2, 6)).reshape(freqs, 2, block_rows, z_n, y_n, block_rows)
    me_y = lax.axis_index("y")
    product = None
    for offset, col_block in ring_blocks(z_cols, "y"):
        row_block = lax.dynamic_index_in_dim(row_panel, (me_y - offset) % y_n, axis=4, keepdims=False)
        part = complex_product(row_block, col_block, "fizk,fzkj->fij")
        product = part if product is None else product + part
    scale_factor = jnp.float32(float(NS) ** (-0.5))
    return product * scale_factor


def solution(mesh):
    fine = Mesh(mesh.devices.reshape(4, 8, 2, 4, 2), SHOT + RECV)
    placed = P(None, None, SHOT, RECV)
    return jax.shard_map(
        per_device,
        mesh=fine,
        in_specs=(placed,),
        out_specs=placed,
        check_vma=False,
    )
```

```python
import jax
import jax.numpy as jnp
from jax import lax
from jax.sharding import Mesh, PartitionSpec as P

NS = 4096
SHOT = ("z_lo", "y")
RECV = ("z_hi", "x", "core")


def complex_product(left_block, right_block, form):
    real_real = jnp.einsum(
        form, left_block[:, 0], right_block[:, 0], preferred_element_type=jnp.float32
    )
    imag_imag = jnp.einsum(
        form, left_block[:, 1], right_block[:, 1], preferred_element_type=jnp.float32
    )
    real_imag = jnp.einsum(
        form, left_block[:, 0], right_block[:, 1], preferred_element_type=jnp.float32
    )
    imag_real = jnp.einsum(
        form, left_block[:, 1], right_block[:, 0], preferred_element_type=jnp.float32
    )
    return jnp.stack((real_real - imag_imag, real_imag + imag_real), axis=1)


def stream_gather(block, axis, wrap):
    n = lax.axis_size(axis)
    axis_size, stride = n, 1
    pos = lax.axis_index(axis)
    k_up = n // 2 if wrap else n - 1
    k_dn = n - 1 - k_up if wrap else n - 1

    def perm(step, direction):
        pairs = []
        for i in range(axis_size):
            p = (i // stride) % n
            q = (p + direction) % n if wrap else p + direction
            origin = p - direction * (step - 1)
            if not wrap and not (0 <= q < n and 0 <= origin < n):
                continue
            pairs.append((i, i + (q - p) * stride))
        return pairs

    ups, dns = [], []
    up = dn = block
    for k in range(1, max(k_up, k_dn) + 1):
        if k <= k_up:
            up = lax.ppermute(up, axis, perm(k, 1))
            ups.append(up)
        if k <= k_dn:
            dn = lax.ppermute(dn, axis, perm(k, -1))
            dns.append(dn)
    stacked = jnp.stack([block] + ups + dns)
    j = jnp.arange(n)
    if wrap:
        d = (pos - j) % n
        sel = jnp.where(d == 0, 0, jnp.where(d <= k_up, d, k_up + n - d))
    else:
        d = pos - j
        sel = jnp.where(d == 0, 0, jnp.where(d > 0, d, k_up - d))
    return jnp.take(stacked, sel, axis=0)


def ring_blocks(block, axis, held):
    n = lax.axis_size(axis)
    right = [(i, (i + 1) % n) for i in range(n)]
    left = [(d, s) for s, d in right]
    got = [(0, block)]
    up = dn = block
    for k in range(1, n // 2 + 1):
        up = lax.ppermute(up, axis, right)
        got.append((k, up))
        if k < n - n // 2:
            dn = lax.ppermute(dn, axis, left)
            got.append((-k, dn))
        if k == 1:
            up, dn, held = lax.optimization_barrier((up, dn, held))
    return got, held


def mirrored_pieces(traces, shot_count, recv_count):
    block_rows = traces.shape[2]
    g = traces.shape[3] // block_rows
    me_shot = lax.axis_index(SHOT)
    pieces = []
    for a in range(g):
        got = []
        for h in range(g):
            perm = [
                (s * recv_count + r, (g * r + h) * recv_count + s // g)
                for s in range(a, shot_count, g)
                for r in range(recv_count)
            ]
            part = traces[:, :, :, h * block_rows:(h + 1) * block_rows]
            got.append(lax.ppermute(part, SHOT + RECV, perm))
        pieces.append(jnp.stack(got)[me_shot % g])
    return jnp.concatenate(pieces, axis=2)


def per_device(traces):
    recv_count = lax.axis_size(RECV)
    shot_count = lax.axis_size(SHOT)
    mirrored = mirrored_pieces(traces, shot_count, recv_count)
    summed = traces.astype(jnp.float32) + jnp.swapaxes(mirrored, 2, 3).astype(jnp.float32)
    averaged = (summed * 0.5).astype(jnp.bfloat16)
    freqs, _, block_rows, col_width = averaged.shape
    rows = stream_gather(averaged, "z_hi", True)
    rows = lax.all_gather(rows, "x", axis=1)
    rows = lax.all_gather(rows, "core", axis=2)
    y_n = lax.axis_size("y")
    z_n = lax.axis_size("z_lo")
    row_panel = jnp.transpose(rows, (3, 4, 5, 0, 1, 2, 6)).reshape(freqs, 2, block_rows, z_n, y_n, block_rows)
    me_y = lax.axis_index("y")
    products = []
    rest = averaged
    for f in range(freqs):
        z_cols = jnp.moveaxis(stream_gather(rest[:1], "z_lo", False), 0, 2)
        z_cols, rest = lax.optimization_barrier((z_cols, rest[1:]))
        blocks, panel = ring_blocks(z_cols, "y", row_panel[f:f + 1])
        product = None
        for offset, col_block in blocks:
            row_block = lax.dynamic_index_in_dim(panel, (me_y - offset) % y_n, axis=4, keepdims=False)
            part = complex_product(row_block, col_block, "fizk,fzkj->fij")
            product = part if product is None else product + part
        products.append(product)
    product = jnp.concatenate(products, axis=0)
    scale_factor = jnp.float32(float(NS) ** (-0.5))
    return product * scale_factor


def solution(mesh):
    fine = Mesh(mesh.devices.reshape(4, 8, 2, 4, 2), SHOT + RECV)
    placed = P(None, None, SHOT, RECV)
    return jax.shard_map(
        per_device,
        mesh=fine,
        in_specs=(placed,),
        out_specs=placed,
        check_vma=False,
    )
```

```python
import jax
import jax.numpy as jnp
from jax import lax
from jax.sharding import Mesh, PartitionSpec as P

NS = 4096
SHOT = ("z_lo", "y")
RECV = ("z_hi", "x", "core")


def complex_product(left_block, right_block, form):
    real_real = jnp.einsum(
        form, left_block[:, 0], right_block[:, 0], preferred_element_type=jnp.float32
    )
    imag_imag = jnp.einsum(
        form, left_block[:, 1], right_block[:, 1], preferred_element_type=jnp.float32
    )
    real_imag = jnp.einsum(
        form, left_block[:, 0], right_block[:, 1], preferred_element_type=jnp.float32
    )
    imag_real = jnp.einsum(
        form, left_block[:, 1], right_block[:, 0], preferred_element_type=jnp.float32
    )
    return jnp.stack((real_real - imag_imag, real_imag + imag_real), axis=1)


def stream_gather(block, axis, wrap):
    n = lax.axis_size(axis)
    axis_size, stride = n, 1
    pos = lax.axis_index(axis)
    k_up = n // 2 if wrap else n - 1
    k_dn = n - 1 - k_up if wrap else n - 1

    def perm(step, direction):
        pairs = []
        for i in range(axis_size):
            p = (i // stride) % n
            q = (p + direction) % n if wrap else p + direction
            origin = p - direction * (step - 1)
            if not wrap and not (0 <= q < n and 0 <= origin < n):
                continue
            pairs.append((i, i + (q - p) * stride))
        return pairs

    ups, dns = [], []
    up = dn = block
    for k in range(1, max(k_up, k_dn) + 1):
        if k <= k_up:
            up = lax.ppermute(up, axis, perm(k, 1))
            ups.append(up)
        if k <= k_dn:
            dn = lax.ppermute(dn, axis, perm(k, -1))
            dns.append(dn)
    stacked = jnp.stack([block] + ups + dns)
    j = jnp.arange(n)
    if wrap:
        d = (pos - j) % n
        sel = jnp.where(d == 0, 0, jnp.where(d <= k_up, d, k_up + n - d))
    else:
        d = pos - j
        sel = jnp.where(d == 0, 0, jnp.where(d > 0, d, k_up - d))
    return jnp.take(stacked, sel, axis=0)


def ring_blocks(block, axis, held):
    n = lax.axis_size(axis)
    right = [(i, (i + 1) % n) for i in range(n)]
    left = [(d, s) for s, d in right]
    got = [(0, block)]
    up = dn = block
    for k in range(1, n // 2 + 1):
        up = lax.ppermute(up, axis, right)
        got.append((k, up))
        if k < n - n // 2:
            dn = lax.ppermute(dn, axis, left)
            got.append((-k, dn))
        if k == 3:
            up, dn, held = lax.optimization_barrier((up, dn, held))
    return got, held


def mirrored_pieces(traces, shot_count, recv_count):
    block_rows = traces.shape[2]
    g = traces.shape[3] // block_rows
    me_shot = lax.axis_index(SHOT)
    pieces = []
    for a in range(g):
        got = []
        for h in range(g):
            perm = [
                (s * recv_count + r, (g * r + h) * recv_count + s // g)
                for s in range(a, shot_count, g)
                for r in range(recv_count)
            ]
            part = traces[:, :, :, h * block_rows:(h + 1) * block_rows]
            got.append(lax.ppermute(part, SHOT + RECV, perm))
        pieces.append(jnp.stack(got)[me_shot % g])
    return jnp.concatenate(pieces, axis=2)


def per_device(traces):
    recv_count = lax.axis_size(RECV)
    shot_count = lax.axis_size(SHOT)
    mirrored = mirrored_pieces(traces, shot_count, recv_count)
    summed = traces.astype(jnp.float32) + jnp.swapaxes(mirrored, 2, 3).astype(jnp.float32)
    averaged = (summed * 0.5).astype(jnp.bfloat16)
    freqs, _, block_rows, col_width = averaged.shape
    rows = stream_gather(averaged, "z_hi", True)
    rows = lax.all_gather(rows, "x", axis=1)
    rows = lax.all_gather(rows, "core", axis=2)
    y_n = lax.axis_size("y")
    z_n = lax.axis_size("z_lo")
    row_panel = jnp.transpose(rows, (3, 4, 5, 0, 1, 2, 6)).reshape(freqs, 2, block_rows, z_n, y_n, block_rows)
    me_y = lax.axis_index("y")
    z_cols = jnp.moveaxis(stream_gather(averaged, "z_lo", False), 0, 2)
    blocks, row_panel = ring_blocks(z_cols, "y", row_panel)
    product = None
    for offset, col_block in blocks:
        row_block = lax.dynamic_index_in_dim(row_panel, (me_y - offset) % y_n, axis=4, keepdims=False)
        part = complex_product(row_block, col_block, "fizk,fzkj->fij")
        product = part if product is None else product + part
    scale_factor = jnp.float32(float(NS) ** (-0.5))
    return product * scale_factor


def solution(mesh):
    fine = Mesh(mesh.devices.reshape(4, 8, 2, 4, 2), SHOT + RECV)
    placed = P(None, None, SHOT, RECV)
    return jax.shard_map(
        per_device,
        mesh=fine,
        in_specs=(placed,),
        out_specs=placed,
        check_vma=False,
    )
```

```python
import jax
import jax.numpy as jnp
from jax import lax
from jax.sharding import Mesh, PartitionSpec as P

NS = 4096
SHOT = ("z_lo", "y")
RECV = ("z_hi", "x", "core")


def complex_product(left_block, right_block, form):
    real_real = jnp.einsum(
        form, left_block[:, 0], right_block[:, 0], preferred_element_type=jnp.float32
    )
    imag_imag = jnp.einsum(
        form, left_block[:, 1], right_block[:, 1], preferred_element_type=jnp.float32
    )
    real_imag = jnp.einsum(
        form, left_block[:, 0], right_block[:, 1], preferred_element_type=jnp.float32
    )
    imag_real = jnp.einsum(
        form, left_block[:, 1], right_block[:, 0], preferred_element_type=jnp.float32
    )
    return jnp.stack((real_real - imag_imag, real_imag + imag_real), axis=1)


def stream_gather(block, axis, wrap):
    n = lax.axis_size(axis)
    axis_size, stride = n, 1
    pos = lax.axis_index(axis)
    k_up = n // 2 if wrap else n - 1
    k_dn = n - 1 - k_up if wrap else n - 1

    def perm(step, direction):
        pairs = []
        for i in range(axis_size):
            p = (i // stride) % n
            q = (p + direction) % n if wrap else p + direction
            origin = p - direction * (step - 1)
            if not wrap and not (0 <= q < n and 0 <= origin < n):
                continue
            pairs.append((i, i + (q - p) * stride))
        return pairs

    ups, dns = [], []
    up = dn = block
    for k in range(1, max(k_up, k_dn) + 1):
        if k <= k_up:
            up = lax.ppermute(up, axis, perm(k, 1))
            ups.append(up)
        if k <= k_dn:
            dn = lax.ppermute(dn, axis, perm(k, -1))
            dns.append(dn)
    stacked = jnp.stack([block] + ups + dns)
    j = jnp.arange(n)
    if wrap:
        d = (pos - j) % n
        sel = jnp.where(d == 0, 0, jnp.where(d <= k_up, d, k_up + n - d))
    else:
        d = pos - j
        sel = jnp.where(d == 0, 0, jnp.where(d > 0, d, k_up - d))
    return jnp.take(stacked, sel, axis=0)


def ring_blocks(block, axis, held):
    n = lax.axis_size(axis)
    right = [(i, (i + 1) % n) for i in range(n)]
    left = [(d, s) for s, d in right]
    got = [(0, block)]
    up = dn = block
    for k in range(1, n // 2 + 1):
        up = lax.ppermute(up, axis, right)
        got.append((k, up))
        if k < n - n // 2:
            dn = lax.ppermute(dn, axis, left)
            got.append((-k, dn))
        if k == 3:
            up, dn, held = lax.optimization_barrier((up, dn, held))
    return got, held


def mirrored_pieces(traces, shot_count, recv_count):
    block_rows = traces.shape[2]
    g = traces.shape[3] // block_rows
    me_shot = lax.axis_index(SHOT)
    pieces = []
    for a in range(g):
        got = []
        for h in range(g):
            perm = [
                (s * recv_count + r, (g * r + h) * recv_count + s // g)
                for s in range(a, shot_count, g)
                for r in range(recv_count)
            ]
            part = traces[:, :, :, h * block_rows:(h + 1) * block_rows]
            got.append(lax.ppermute(part, SHOT + RECV, perm))
        pieces.append(jnp.stack(got)[me_shot % g])
    return jnp.concatenate(pieces, axis=2)


def per_device(traces):
    recv_count = lax.axis_size(RECV)
    shot_count = lax.axis_size(SHOT)
    mirrored = mirrored_pieces(traces, shot_count, recv_count)
    summed = traces.astype(jnp.float32) + jnp.swapaxes(mirrored, 2, 3).astype(jnp.float32)
    averaged = (summed * 0.5).astype(jnp.bfloat16)
    freqs, _, block_rows, col_width = averaged.shape
    rows = lax.all_gather(averaged, ("z_hi", "x"), axis=0)
    rows = lax.all_gather(rows, "core", axis=1)
    y_n = lax.axis_size("y")
    z_n = lax.axis_size("z_lo")
    row_panel = jnp.transpose(rows, (2, 3, 4, 0, 1, 5)).reshape(freqs, 2, block_rows, z_n, y_n, block_rows)
    me_y = lax.axis_index("y")
    z_cols = jnp.moveaxis(stream_gather(averaged, "z_lo", False), 0, 2)
    blocks, row_panel = ring_blocks(z_cols, "y", row_panel)
    product = None
    for offset, col_block in blocks:
        row_block = lax.dynamic_index_in_dim(row_panel, (me_y - offset) % y_n, axis=4, keepdims=False)
        part = complex_product(row_block, col_block, "fizk,fzkj->fij")
        product = part if product is None else product + part
    scale_factor = jnp.float32(float(NS) ** (-0.5))
    return product * scale_factor


def solution(mesh):
    fine = Mesh(mesh.devices.reshape(4, 8, 2, 4, 2), SHOT + RECV)
    placed = P(None, None, SHOT, RECV)
    return jax.shard_map(
        per_device,
        mesh=fine,
        in_specs=(placed,),
        out_specs=placed,
        check_vma=False,
    )
```

```python
import jax
import jax.numpy as jnp
from jax import lax
from jax.sharding import Mesh, PartitionSpec as P

NS = 4096
SHOT = ("z_lo", "y")
RECV = ("z_hi", "x", "core")


def complex_product(left_block, right_block, form):
    real_real = jnp.einsum(
        form, left_block[:, 0], right_block[:, 0], preferred_element_type=jnp.float32
    )
    imag_imag = jnp.einsum(
        form, left_block[:, 1], right_block[:, 1], preferred_element_type=jnp.float32
    )
    real_imag = jnp.einsum(
        form, left_block[:, 0], right_block[:, 1], preferred_element_type=jnp.float32
    )
    imag_real = jnp.einsum(
        form, left_block[:, 1], right_block[:, 0], preferred_element_type=jnp.float32
    )
    return jnp.stack((real_real - imag_imag, real_imag + imag_real), axis=1)


def stream_gather(block, axis, wrap):
    n = lax.axis_size(axis)
    axis_size, stride = n, 1
    pos = lax.axis_index(axis)
    k_up = n // 2 if wrap else n - 1
    k_dn = n - 1 - k_up if wrap else n - 1

    def perm(step, direction):
        pairs = []
        for i in range(axis_size):
            p = (i // stride) % n
            q = (p + direction) % n if wrap else p + direction
            origin = p - direction * (step - 1)
            if not wrap and not (0 <= q < n and 0 <= origin < n):
                continue
            pairs.append((i, i + (q - p) * stride))
        return pairs

    ups, dns = [], []
    up = dn = block
    for k in range(1, max(k_up, k_dn) + 1):
        if k <= k_up:
            up = lax.ppermute(up, axis, perm(k, 1))
            ups.append(up)
        if k <= k_dn:
            dn = lax.ppermute(dn, axis, perm(k, -1))
            dns.append(dn)
    stacked = jnp.stack([block] + ups + dns)
    j = jnp.arange(n)
    if wrap:
        d = (pos - j) % n
        sel = jnp.where(d == 0, 0, jnp.where(d <= k_up, d, k_up + n - d))
    else:
        d = pos - j
        sel = jnp.where(d == 0, 0, jnp.where(d > 0, d, k_up - d))
    return jnp.take(stacked, sel, axis=0)


def ring_blocks(block, axis, held):
    n = lax.axis_size(axis)
    right = [(i, (i + 1) % n) for i in range(n)]
    left = [(d, s) for s, d in right]
    got = [(0, block)]
    up = dn = block
    for k in range(1, n // 2 + 1):
        up = lax.ppermute(up, axis, right)
        got.append((k, up))
        if k < n - n // 2:
            dn = lax.ppermute(dn, axis, left)
            got.append((-k, dn))
        if k == 3:
            up, dn, held = lax.optimization_barrier((up, dn, held))
    return got, held


def z_hi_swap(block):
    z_axes = ("z_lo", "z_hi")
    lo_n = lax.axis_size("z_lo")
    n = lax.axis_size(z_axes)

    def at(z):
        z %= n
        return (z % lo_n) * (n // lo_n) + z // lo_n

    ahead = [(at(z), at(z + 2)) for z in range(n)]
    behind = [(at(z), at(z - 2)) for z in range(n)]
    half = block.shape[0] // 2
    one, other = block[:half], block[half:]
    for _ in range(2):
        one = lax.ppermute(one, z_axes, ahead)
        other = lax.ppermute(other, z_axes, behind)
    partner = jnp.concatenate((one, other), axis=0)
    low = lax.axis_index("z_hi") == 0
    return jnp.stack((jnp.where(low, block, partner), jnp.where(low, partner, block)))


def mirrored_pieces(traces, shot_count, recv_count):
    block_rows = traces.shape[2]
    g = traces.shape[3] // block_rows
    me_shot = lax.axis_index(SHOT)
    pieces = []
    for a in range(g):
        got = []
        for h in range(g):
            perm = [
                (s * recv_count + r, (g * r + h) * recv_count + s // g)
                for s in range(a, shot_count, g)
                for r in range(recv_count)
            ]
            part = traces[:, :, :, h * block_rows:(h + 1) * block_rows]
            got.append(lax.ppermute(part, SHOT + RECV, perm))
        pieces.append(jnp.stack(got)[me_shot % g])
    return jnp.concatenate(pieces, axis=2)


def per_device(traces):
    recv_count = lax.axis_size(RECV)
    shot_count = lax.axis_size(SHOT)
    mirrored = mirrored_pieces(traces, shot_count, recv_count)
    summed = traces.astype(jnp.float32) + jnp.swapaxes(mirrored, 2, 3).astype(jnp.float32)
    averaged = (summed * 0.5).astype(jnp.bfloat16)
    freqs, _, block_rows, col_width = averaged.shape
    rows = z_hi_swap(averaged)
    rows = lax.all_gather(rows, "x", axis=1)
    rows = lax.all_gather(rows, "core", axis=2)
    y_n = lax.axis_size("y")
    z_n = lax.axis_size("z_lo")
    row_panel = jnp.transpose(rows, (3, 4, 5, 0, 1, 2, 6)).reshape(freqs, 2, block_rows, z_n, y_n, block_rows)
    me_y = lax.axis_index("y")
    z_cols = jnp.moveaxis(stream_gather(averaged, "z_lo", False), 0, 2)
    blocks, row_panel = ring_blocks(z_cols, "y", row_panel)
    product = None
    for offset, col_block in blocks:
        row_block = lax.dynamic_index_in_dim(row_panel, (me_y - offset) % y_n, axis=4, keepdims=False)
        part = complex_product(row_block, col_block, "fizk,fzkj->fij")
        product = part if product is None else product + part
    scale_factor = jnp.float32(float(NS) ** (-0.5))
    return product * scale_factor


def solution(mesh):
    fine = Mesh(mesh.devices.reshape(4, 8, 2, 4, 2), SHOT + RECV)
    placed = P(None, None, SHOT, RECV)
    return jax.shard_map(
        per_device,
        mesh=fine,
        in_specs=(placed,),
        out_specs=placed,
        check_vma=False,
    )
```

```python
import jax
import jax.numpy as jnp
from jax import lax
from jax.sharding import Mesh, PartitionSpec as P

NS = 4096
SHOT = ("z_lo", "y")
RECV = ("z_hi", "x", "core")


def complex_product(left_block, right_block, form):
    real_real = jnp.einsum(
        form, left_block[:, 0], right_block[:, 0], preferred_element_type=jnp.float32
    )
    imag_imag = jnp.einsum(
        form, left_block[:, 1], right_block[:, 1], preferred_element_type=jnp.float32
    )
    real_imag = jnp.einsum(
        form, left_block[:, 0], right_block[:, 1], preferred_element_type=jnp.float32
    )
    imag_real = jnp.einsum(
        form, left_block[:, 1], right_block[:, 0], preferred_element_type=jnp.float32
    )
    return jnp.stack((real_real - imag_imag, real_imag + imag_real), axis=1)


def stream_gather(block, axis, wrap):
    n = lax.axis_size(axis)
    axis_size, stride = n, 1
    pos = lax.axis_index(axis)
    k_up = n // 2 if wrap else n - 1
    k_dn = n - 1 - k_up if wrap else n - 1

    def perm(step, direction):
        pairs = []
        for i in range(axis_size):
            p = (i // stride) % n
            q = (p + direction) % n if wrap else p + direction
            origin = p - direction * (step - 1)
            if not wrap and not (0 <= q < n and 0 <= origin < n):
                continue
            pairs.append((i, i + (q - p) * stride))
        return pairs

    ups, dns = [], []
    up = dn = block
    for k in range(1, max(k_up, k_dn) + 1):
        if k <= k_up:
            up = lax.ppermute(up, axis, perm(k, 1))
            ups.append(up)
        if k <= k_dn:
            dn = lax.ppermute(dn, axis, perm(k, -1))
            dns.append(dn)
    stacked = jnp.stack([block] + ups + dns)
    j = jnp.arange(n)
    if wrap:
        d = (pos - j) % n
        sel = jnp.where(d == 0, 0, jnp.where(d <= k_up, d, k_up + n - d))
    else:
        d = pos - j
        sel = jnp.where(d == 0, 0, jnp.where(d > 0, d, k_up - d))
    return jnp.take(stacked, sel, axis=0)


def ring_blocks(block, axis, held):
    n = lax.axis_size(axis)
    right = [(i, (i + 1) % n) for i in range(n)]
    left = [(d, s) for s, d in right]
    got = [(0, block)]
    up = dn = block
    for k in range(1, n // 2 + 1):
        up = lax.ppermute(up, axis, right)
        got.append((k, up))
        if k < n - n // 2:
            dn = lax.ppermute(dn, axis, left)
            got.append((-k, dn))
        if k == 3:
            up, dn, held = lax.optimization_barrier((up, dn, held))
    return got, held


def z_hi_swap(block):
    z_axes = ("z_lo", "z_hi")
    lo_n = lax.axis_size("z_lo")
    n = lax.axis_size(z_axes)

    def at(z):
        z %= n
        return (z % lo_n) * (n // lo_n) + z // lo_n

    ahead = [(at(z), at(z + 2)) for z in range(n)]
    behind = [(at(z), at(z - 2)) for z in range(n)]
    half = block.shape[0] // 2
    one, other = block[:half], block[half:]
    for _ in range(2):
        one = lax.ppermute(one, z_axes, ahead)
        other = lax.ppermute(other, z_axes, behind)
    partner = jnp.concatenate((one, other), axis=0)
    low = lax.axis_index("z_hi") == 0
    return jnp.stack((jnp.where(low, block, partner), jnp.where(low, partner, block)))


def mirrored_pieces(traces, shot_count, recv_count):
    block_rows = traces.shape[2]
    g = traces.shape[3] // block_rows
    me_shot = lax.axis_index(SHOT)
    pieces = []
    for a in range(g):
        got = []
        for h in range(g):
            perm = [
                (s * recv_count + r, (g * r + h) * recv_count + s // g)
                for s in range(a, shot_count, g)
                for r in range(recv_count)
            ]
            part = traces[:, :, :, h * block_rows:(h + 1) * block_rows]
            got.append(lax.ppermute(part, SHOT + RECV, perm))
        pieces.append(jnp.stack(got)[me_shot % g])
    return jnp.concatenate(pieces, axis=2)


def per_device(traces):
    recv_count = lax.axis_size(RECV)
    shot_count = lax.axis_size(SHOT)
    mirrored = mirrored_pieces(traces, shot_count, recv_count)
    summed = traces.astype(jnp.float32) + jnp.swapaxes(mirrored, 2, 3).astype(jnp.float32)
    averaged = (summed * 0.5).astype(jnp.bfloat16)
    freqs, _, block_rows, col_width = averaged.shape
    rows = z_hi_swap(averaged)
    rows = lax.all_gather(rows, "x", axis=1)
    rows = lax.all_gather(rows, "core", axis=2)
    y_n = lax.axis_size("y")
    z_n = lax.axis_size("z_lo")
    row_panel = jnp.transpose(rows, (3, 4, 5, 0, 1, 2, 6)).reshape(freqs, 2, block_rows, z_n, y_n, block_rows)
    me_y = lax.axis_index("y")
    z_first = jnp.moveaxis(stream_gather(averaged[:1], "z_lo", False), 0, 2)
    blocks, row_panel = ring_blocks(z_first, "y", row_panel)
    product = None
    for offset, col_block in blocks:
        row_block = lax.dynamic_index_in_dim(row_panel[:1], (me_y - offset) % y_n, axis=4, keepdims=False)
        part = complex_product(row_block, col_block, "fizk,fzkj->fij")
        product = part if product is None else product + part
    y_blocks, _ = ring_blocks(averaged[1:], "y", averaged[1:])
    y_first = stream_gather(jnp.stack([block for _, block in y_blocks], axis=0), "z_lo", False)
    late = None
    for t, (offset, _) in enumerate(y_blocks):
        row_block = lax.dynamic_index_in_dim(row_panel[1:], (me_y - offset) % y_n, axis=4, keepdims=False)
        part = complex_product(row_block, jnp.moveaxis(y_first[:, t], 0, 2), "fizk,fzkj->fij")
        late = part if late is None else late + part
    product = jnp.concatenate((product, late), axis=0)
    scale_factor = jnp.float32(float(NS) ** (-0.5))
    return product * scale_factor


def solution(mesh):
    fine = Mesh(mesh.devices.reshape(4, 8, 2, 4, 2), SHOT + RECV)
    placed = P(None, None, SHOT, RECV)
    return jax.shard_map(
        per_device,
        mesh=fine,
        in_specs=(placed,),
        out_specs=placed,
        check_vma=False,
    )
```

```python
import jax
import jax.numpy as jnp
from jax import lax
from jax.sharding import Mesh, PartitionSpec as P

NS = 4096
SHOT = ("z_lo", "y")
RECV = ("z_hi", "x", "core")


def complex_product(left_block, right_block, form):
    real_real = jnp.einsum(
        form, left_block[:, 0], right_block[:, 0], preferred_element_type=jnp.float32
    )
    imag_imag = jnp.einsum(
        form, left_block[:, 1], right_block[:, 1], preferred_element_type=jnp.float32
    )
    real_imag = jnp.einsum(
        form, left_block[:, 0], right_block[:, 1], preferred_element_type=jnp.float32
    )
    imag_real = jnp.einsum(
        form, left_block[:, 1], right_block[:, 0], preferred_element_type=jnp.float32
    )
    return jnp.stack((real_real - imag_imag, real_imag + imag_real), axis=1)


def stream_gather(block, axis, wrap):
    n = lax.axis_size(axis)
    axis_size, stride = n, 1
    pos = lax.axis_index(axis)
    k_up = n // 2 if wrap else n - 1
    k_dn = n - 1 - k_up if wrap else n - 1

    def perm(step, direction):
        pairs = []
        for i in range(axis_size):
            p = (i // stride) % n
            q = (p + direction) % n if wrap else p + direction
            origin = p - direction * (step - 1)
            if not wrap and not (0 <= q < n and 0 <= origin < n):
                continue
            pairs.append((i, i + (q - p) * stride))
        return pairs

    ups, dns = [], []
    up = dn = block
    for k in range(1, max(k_up, k_dn) + 1):
        if k <= k_up:
            up = lax.ppermute(up, axis, perm(k, 1))
            ups.append(up)
        if k <= k_dn:
            dn = lax.ppermute(dn, axis, perm(k, -1))
            dns.append(dn)
    stacked = jnp.stack([block] + ups + dns)
    j = jnp.arange(n)
    if wrap:
        d = (pos - j) % n
        sel = jnp.where(d == 0, 0, jnp.where(d <= k_up, d, k_up + n - d))
    else:
        d = pos - j
        sel = jnp.where(d == 0, 0, jnp.where(d > 0, d, k_up - d))
    return jnp.take(stacked, sel, axis=0)


def ring_blocks(block, axis, held):
    n = lax.axis_size(axis)
    right = [(i, (i + 1) % n) for i in range(n)]
    left = [(d, s) for s, d in right]
    got = [(0, block)]
    up = dn = block
    for k in range(1, n // 2 + 1):
        up = lax.ppermute(up, axis, right)
        got.append((k, up))
        if k < n - n // 2:
            dn = lax.ppermute(dn, axis, left)
            got.append((-k, dn))
        if k == 3:
            up, dn, held = lax.optimization_barrier((up, dn, held))
    return got, held


def mirrored_pieces(traces, shot_count, recv_count):
    block_rows = traces.shape[2]
    g = traces.shape[3] // block_rows
    me_shot = lax.axis_index(SHOT)
    pieces = []
    for a in range(g):
        got = []
        for h in range(g):
            perm = [
                (s * recv_count + r, (g * r + h) * recv_count + s // g)
                for s in range(a, shot_count, g)
                for r in range(recv_count)
            ]
            part = traces[:, :, :, h * block_rows:(h + 1) * block_rows]
            got.append(lax.ppermute(part, SHOT + RECV, perm))
        pieces.append(jnp.stack(got)[me_shot % g])
    return jnp.concatenate(pieces, axis=2)


def per_device(traces):
    recv_count = lax.axis_size(RECV)
    shot_count = lax.axis_size(SHOT)
    mirrored = mirrored_pieces(traces, shot_count, recv_count)
    summed = traces.astype(jnp.float32) + jnp.swapaxes(mirrored, 2, 3).astype(jnp.float32)
    averaged = (summed * 0.5).astype(jnp.bfloat16)
    freqs, _, block_rows, col_width = averaged.shape
    rows = stream_gather(averaged, "z_hi", True)
    rows = lax.all_gather(rows, "x", axis=1)
    rows = lax.all_gather(rows, "core", axis=2)
    y_n = lax.axis_size("y")
    z_n = lax.axis_size("z_lo")
    row_panel = jnp.transpose(rows, (3, 4, 5, 0, 1, 2, 6)).reshape(freqs, 2, block_rows, z_n, y_n, block_rows)
    me_y = lax.axis_index("y")
    z_cols = jnp.moveaxis(stream_gather(averaged, "z_lo", False), 0, 2)
    blocks, row_panel = ring_blocks(z_cols, "y", row_panel)
    real, imag = row_panel[:, 0], row_panel[:, 1]
    paired = jnp.stack((jnp.stack((real, -imag), axis=1), jnp.stack((imag, real), axis=1)), axis=1)
    product = None
    for offset, col_block in blocks:
        row_block = lax.dynamic_index_in_dim(paired, (me_y - offset) % y_n, axis=5, keepdims=False)
        part = jnp.einsum("fgcizk,fczkj->fgij", row_block, col_block, preferred_element_type=jnp.float32)
        product = part if product is None else product + part
    scale_factor = jnp.float32(float(NS) ** (-0.5))
    return product * scale_factor


def solution(mesh):
    fine = Mesh(mesh.devices.reshape(4, 8, 2, 4, 2), SHOT + RECV)
    placed = P(None, None, SHOT, RECV)
    return jax.shard_map(
        per_device,
        mesh=fine,
        in_specs=(placed,),
        out_specs=placed,
        check_vma=False,
    )
```

```python
import jax
import jax.numpy as jnp
from jax import lax
from jax.sharding import Mesh, PartitionSpec as P

NS = 4096
SHOT = ("z_lo", "y")
RECV = ("z_hi", "x", "core")


def complex_product(left_block, right_block, form):
    real_real = jnp.einsum(
        form, left_block[:, 0], right_block[:, 0], preferred_element_type=jnp.float32
    )
    imag_imag = jnp.einsum(
        form, left_block[:, 1], right_block[:, 1], preferred_element_type=jnp.float32
    )
    real_imag = jnp.einsum(
        form, left_block[:, 0], right_block[:, 1], preferred_element_type=jnp.float32
    )
    imag_real = jnp.einsum(
        form, left_block[:, 1], right_block[:, 0], preferred_element_type=jnp.float32
    )
    return jnp.stack((real_real - imag_imag, real_imag + imag_real), axis=1)


def stream_gather(block, axis, wrap):
    n = lax.axis_size(axis)
    axis_size, stride = n, 1
    pos = lax.axis_index(axis)
    k_up = n // 2 if wrap else n - 1
    k_dn = n - 1 - k_up if wrap else n - 1

    def perm(step, direction):
        pairs = []
        for i in range(axis_size):
            p = (i // stride) % n
            q = (p + direction) % n if wrap else p + direction
            origin = p - direction * (step - 1)
            if not wrap and not (0 <= q < n and 0 <= origin < n):
                continue
            pairs.append((i, i + (q - p) * stride))
        return pairs

    ups, dns = [], []
    up = dn = block
    for k in range(1, max(k_up, k_dn) + 1):
        if k <= k_up:
            up = lax.ppermute(up, axis, perm(k, 1))
            ups.append(up)
        if k <= k_dn:
            dn = lax.ppermute(dn, axis, perm(k, -1))
            dns.append(dn)
    stacked = jnp.stack([block] + ups + dns)
    j = jnp.arange(n)
    if wrap:
        d = (pos - j) % n
        sel = jnp.where(d == 0, 0, jnp.where(d <= k_up, d, k_up + n - d))
    else:
        d = pos - j
        sel = jnp.where(d == 0, 0, jnp.where(d > 0, d, k_up - d))
    return jnp.take(stacked, sel, axis=0)


def ring_blocks(block, axis, held):
    n = lax.axis_size(axis)
    right = [(i, (i + 1) % n) for i in range(n)]
    left = [(d, s) for s, d in right]
    got = [(0, block)]
    up = dn = block
    for k in range(1, n // 2 + 1):
        up = lax.ppermute(up, axis, right)
        got.append((k, up))
        if k < n - n // 2:
            dn = lax.ppermute(dn, axis, left)
            got.append((-k, dn))
        if k == n // 2:
            up, dn, held = lax.optimization_barrier((up, dn, held))
    return got, held


def mirrored_pieces(traces, shot_count, recv_count):
    block_rows = traces.shape[2]
    g = traces.shape[3] // block_rows
    me_shot = lax.axis_index(SHOT)
    pieces = []
    for a in range(g):
        got = []
        for h in range(g):
            perm = [
                (s * recv_count + r, (g * r + h) * recv_count + s // g)
                for s in range(a, shot_count, g)
                for r in range(recv_count)
            ]
            part = traces[:, :, :, h * block_rows:(h + 1) * block_rows]
            got.append(lax.ppermute(part, SHOT + RECV, perm))
        pieces.append(jnp.stack(got)[me_shot % g])
    return jnp.concatenate(pieces, axis=2)


def per_device(traces):
    recv_count = lax.axis_size(RECV)
    shot_count = lax.axis_size(SHOT)
    mirrored = mirrored_pieces(traces, shot_count, recv_count)
    summed = traces.astype(jnp.float32) + jnp.swapaxes(mirrored, 2, 3).astype(jnp.float32)
    averaged = (summed * 0.5).astype(jnp.bfloat16)
    freqs, _, block_rows, col_width = averaged.shape
    rows = stream_gather(averaged, "z_hi", True)
    rows = lax.all_gather(rows, "x", axis=1)
    rows = lax.all_gather(rows, "core", axis=2)
    y_n = lax.axis_size("y")
    z_n = lax.axis_size("z_lo")
    row_panel = jnp.transpose(rows, (3, 4, 5, 0, 1, 2, 6)).reshape(freqs, 2, block_rows, z_n, y_n, block_rows)
    me_y = lax.axis_index("y")
    z_cols = jnp.moveaxis(stream_gather(averaged, "z_lo", False), 0, 2)
    blocks, row_panel = ring_blocks(z_cols, "y", row_panel)
    real, imag = row_panel[:, 0], row_panel[:, 1]
    paired = jnp.stack((jnp.stack((real, -imag), axis=1), jnp.stack((imag, real), axis=1)), axis=1)
    product = None
    for offset, col_block in blocks:
        row_block = lax.dynamic_index_in_dim(paired, (me_y - offset) % y_n, axis=5, keepdims=False)
        part = jnp.einsum("fgcizk,fczkj->fgij", row_block, col_block, preferred_element_type=jnp.float32)
        product = part if product is None else product + part
    scale_factor = jnp.float32(float(NS) ** (-0.5))
    return product * scale_factor


def solution(mesh):
    fine = Mesh(mesh.devices.reshape(4, 8, 2, 4, 2), SHOT + RECV)
    placed = P(None, None, SHOT, RECV)
    return jax.shard_map(
        per_device,
        mesh=fine,
        in_specs=(placed,),
        out_specs=placed,
        check_vma=False,
    )
```

```python
import jax
import jax.numpy as jnp
from jax import lax
from jax.sharding import Mesh, PartitionSpec as P

NS = 4096
SHOT = ("z_lo", "y")
RECV = ("z_hi", "x", "core")


def complex_product(left_block, right_block, form):
    real_real = jnp.einsum(
        form, left_block[:, 0], right_block[:, 0], preferred_element_type=jnp.float32
    )
    imag_imag = jnp.einsum(
        form, left_block[:, 1], right_block[:, 1], preferred_element_type=jnp.float32
    )
    real_imag = jnp.einsum(
        form, left_block[:, 0], right_block[:, 1], preferred_element_type=jnp.float32
    )
    imag_real = jnp.einsum(
        form, left_block[:, 1], right_block[:, 0], preferred_element_type=jnp.float32
    )
    return jnp.stack((real_real - imag_imag, real_imag + imag_real), axis=1)


def stream_gather(block, axis, wrap):
    n = lax.axis_size(axis)
    axis_size, stride = n, 1
    pos = lax.axis_index(axis)
    k_up = n // 2 if wrap else n - 1
    k_dn = n - 1 - k_up if wrap else n - 1

    def perm(step, direction):
        pairs = []
        for i in range(axis_size):
            p = (i // stride) % n
            q = (p + direction) % n if wrap else p + direction
            origin = p - direction * (step - 1)
            if not wrap and not (0 <= q < n and 0 <= origin < n):
                continue
            pairs.append((i, i + (q - p) * stride))
        return pairs

    ups, dns = [], []
    up = dn = block
    for k in range(1, max(k_up, k_dn) + 1):
        if k <= k_up:
            up = lax.ppermute(up, axis, perm(k, 1))
            ups.append(up)
        if k <= k_dn:
            dn = lax.ppermute(dn, axis, perm(k, -1))
            dns.append(dn)
    stacked = jnp.stack([block] + ups + dns)
    j = jnp.arange(n)
    if wrap:
        d = (pos - j) % n
        sel = jnp.where(d == 0, 0, jnp.where(d <= k_up, d, k_up + n - d))
    else:
        d = pos - j
        sel = jnp.where(d == 0, 0, jnp.where(d > 0, d, k_up - d))
    return jnp.take(stacked, sel, axis=0)


def ring_blocks(block, axis, held):
    n = lax.axis_size(axis)
    right = [(i, (i + 1) % n) for i in range(n)]
    left = [(d, s) for s, d in right]
    got = [(0, block)]
    up = dn = block
    for k in range(1, n // 2 + 1):
        up = lax.ppermute(up, axis, right)
        got.append((k, up))
        if k < n - n // 2:
            dn = lax.ppermute(dn, axis, left)
            got.append((-k, dn))
        if k == 3:
            up, dn, held = lax.optimization_barrier((up, dn, held))
    return got, held


def mirrored_pieces(traces, shot_count, recv_count):
    block_rows = traces.shape[2]
    g = traces.shape[3] // block_rows
    me_shot = lax.axis_index(SHOT)
    pieces = []
    for a in range(g):
        got = []
        for h in range(g):
            perm = [
                (s * recv_count + r, (g * r + h) * recv_count + s // g)
                for s in range(a, shot_count, g)
                for r in range(recv_count)
            ]
            part = traces[:, :, :, h * block_rows:(h + 1) * block_rows]
            got.append(lax.ppermute(part, SHOT + RECV, perm))
        pieces.append(jnp.stack(got)[me_shot % g])
    return jnp.concatenate(pieces, axis=2)


def per_device(traces):
    recv_count = lax.axis_size(RECV)
    shot_count = lax.axis_size(SHOT)
    mirrored = mirrored_pieces(traces, shot_count, recv_count)
    summed = traces.astype(jnp.float32) + jnp.swapaxes(mirrored, 2, 3).astype(jnp.float32)
    averaged = (summed * 0.5).astype(jnp.bfloat16)
    freqs, _, block_rows, col_width = averaged.shape
    rows = stream_gather(averaged, "z_hi", True)
    rows = lax.all_gather(rows, "x", axis=1)
    rows = lax.all_gather(rows, "core", axis=2)
    y_n = lax.axis_size("y")
    z_n = lax.axis_size("z_lo")
    row_panel = jnp.transpose(rows, (3, 4, 5, 0, 1, 2, 6)).reshape(freqs, 2, block_rows, z_n, y_n, block_rows)
    me_y = lax.axis_index("y")
    z_cols = jnp.moveaxis(stream_gather(averaged, "z_lo", False), 0, 2)
    blocks, row_panel = ring_blocks(z_cols, "y", row_panel)
    real, imag = row_panel[:, 0], row_panel[:, 1]
    paired = jnp.stack((jnp.stack((real, -imag), axis=1), jnp.stack((imag, real), axis=1)), axis=1)
    paired = jnp.transpose(paired, (5, 0, 1, 2, 4, 3, 6))
    product = None
    for offset, col_block in blocks:
        row_block = lax.dynamic_index_in_dim(paired, (me_y - offset) % y_n, axis=0, keepdims=False)
        part = jnp.einsum("fgczik,fczkj->fgij", row_block, col_block, preferred_element_type=jnp.float32)
        product = part if product is None else product + part
    scale_factor = jnp.float32(float(NS) ** (-0.5))
    return product * scale_factor


def solution(mesh):
    fine = Mesh(mesh.devices.reshape(4, 8, 2, 4, 2), SHOT + RECV)
    placed = P(None, None, SHOT, RECV)
    return jax.shard_map(
        per_device,
        mesh=fine,
        in_specs=(placed,),
        out_specs=placed,
        check_vma=False,
    )
```

```python
import jax
import jax.numpy as jnp
from jax import lax
from jax.sharding import Mesh, PartitionSpec as P

NS = 4096
SHOT = ("z_lo", "y")
RECV = ("z_hi", "x", "core")


def complex_product(left_block, right_block, form):
    real_real = jnp.einsum(
        form, left_block[:, 0], right_block[:, 0], preferred_element_type=jnp.float32
    )
    imag_imag = jnp.einsum(
        form, left_block[:, 1], right_block[:, 1], preferred_element_type=jnp.float32
    )
    real_imag = jnp.einsum(
        form, left_block[:, 0], right_block[:, 1], preferred_element_type=jnp.float32
    )
    imag_real = jnp.einsum(
        form, left_block[:, 1], right_block[:, 0], preferred_element_type=jnp.float32
    )
    return jnp.stack((real_real - imag_imag, real_imag + imag_real), axis=1)


def stream_gather(block, axis, wrap):
    n = lax.axis_size(axis)
    axis_size, stride = n, 1
    pos = lax.axis_index(axis)
    k_up = n // 2 if wrap else n - 1
    k_dn = n - 1 - k_up if wrap else n - 1

    def perm(step, direction):
        pairs = []
        for i in range(axis_size):
            p = (i // stride) % n
            q = (p + direction) % n if wrap else p + direction
            origin = p - direction * (step - 1)
            if not wrap and not (0 <= q < n and 0 <= origin < n):
                continue
            pairs.append((i, i + (q - p) * stride))
        return pairs

    ups, dns = [], []
    up = dn = block
    for k in range(1, max(k_up, k_dn) + 1):
        if k <= k_up:
            up = lax.ppermute(up, axis, perm(k, 1))
            ups.append(up)
        if k <= k_dn:
            dn = lax.ppermute(dn, axis, perm(k, -1))
            dns.append(dn)
    stacked = jnp.stack([block] + ups + dns)
    j = jnp.arange(n)
    if wrap:
        d = (pos - j) % n
        sel = jnp.where(d == 0, 0, jnp.where(d <= k_up, d, k_up + n - d))
    else:
        d = pos - j
        sel = jnp.where(d == 0, 0, jnp.where(d > 0, d, k_up - d))
    return jnp.take(stacked, sel, axis=0)


def ring_blocks(block, axis, held):
    n = lax.axis_size(axis)
    right = [(i, (i + 1) % n) for i in range(n)]
    left = [(d, s) for s, d in right]
    got = [(0, block)]
    up = dn = block
    for k in range(1, n // 2 + 1):
        up = lax.ppermute(up, axis, right)
        got.append((k, up))
        if k < n - n // 2:
            dn = lax.ppermute(dn, axis, left)
            got.append((-k, dn))
        if k == 0:
            up, dn, held = lax.optimization_barrier((up, dn, held))
    return got, held


def mirrored_pieces(traces, shot_count, recv_count):
    block_rows = traces.shape[2]
    g = traces.shape[3] // block_rows
    me_shot = lax.axis_index(SHOT)
    pieces = []
    for a in range(g):
        got = []
        for h in range(g):
            perm = [
                (s * recv_count + r, (g * r + h) * recv_count + s // g)
                for s in range(a, shot_count, g)
                for r in range(recv_count)
            ]
            part = traces[:, :, :, h * block_rows:(h + 1) * block_rows]
            got.append(lax.ppermute(part, SHOT + RECV, perm))
        pieces.append(jnp.stack(got)[me_shot % g])
    return jnp.concatenate(pieces, axis=2)


def per_device(traces):
    recv_count = lax.axis_size(RECV)
    shot_count = lax.axis_size(SHOT)
    mirrored = mirrored_pieces(traces, shot_count, recv_count)
    summed = traces.astype(jnp.float32) + jnp.swapaxes(mirrored, 2, 3).astype(jnp.float32)
    averaged = (summed * 0.5).astype(jnp.bfloat16)
    freqs, _, block_rows, col_width = averaged.shape
    rows = stream_gather(averaged, "z_hi", True)
    rows = lax.all_gather(rows, "x", axis=1)
    rows = lax.all_gather(rows, "core", axis=2)
    y_n = lax.axis_size("y")
    z_n = lax.axis_size("z_lo")
    row_panel = jnp.transpose(rows, (3, 4, 5, 0, 1, 2, 6)).reshape(freqs, 2, block_rows, z_n, y_n, block_rows)
    me_y = lax.axis_index("y")
    z_cols = jnp.moveaxis(stream_gather(averaged, "z_lo", False), 0, 2)
    blocks, row_panel = ring_blocks(z_cols, "y", row_panel)
    real, imag = row_panel[:, 0], row_panel[:, 1]
    paired = jnp.stack((jnp.stack((real, -imag), axis=1), jnp.stack((imag, real), axis=1)), axis=1)
    paired = jnp.transpose(paired, (5, 0, 1, 2, 4, 3, 6))
    product = None
    for offset, col_block in blocks:
        row_block = lax.dynamic_index_in_dim(paired, (me_y - offset) % y_n, axis=0, keepdims=False)
        part = jnp.einsum("fgczik,fczkj->fgij", row_block, col_block, preferred_element_type=jnp.float32)
        product = part if product is None else product + part
    scale_factor = jnp.float32(float(NS) ** (-0.5))
    return product * scale_factor


def solution(mesh):
    fine = Mesh(mesh.devices.reshape(4, 8, 2, 4, 2), SHOT + RECV)
    placed = P(None, None, SHOT, RECV)
    return jax.shard_map(
        per_device,
        mesh=fine,
        in_specs=(placed,),
        out_specs=placed,
        check_vma=False,
    )
```

```python
import jax
import jax.numpy as jnp
from jax import lax
from jax.sharding import Mesh, PartitionSpec as P

NS = 4096
SHOT = ("z_lo", "y")
RECV = ("z_hi", "x", "core")


def complex_product(left_block, right_block, form):
    real_real = jnp.einsum(
        form, left_block[:, 0], right_block[:, 0], preferred_element_type=jnp.float32
    )
    imag_imag = jnp.einsum(
        form, left_block[:, 1], right_block[:, 1], preferred_element_type=jnp.float32
    )
    real_imag = jnp.einsum(
        form, left_block[:, 0], right_block[:, 1], preferred_element_type=jnp.float32
    )
    imag_real = jnp.einsum(
        form, left_block[:, 1], right_block[:, 0], preferred_element_type=jnp.float32
    )
    return jnp.stack((real_real - imag_imag, real_imag + imag_real), axis=1)


def stream_gather(block, axis, wrap):
    n = lax.axis_size(axis)
    axis_size, stride = n, 1
    pos = lax.axis_index(axis)
    k_up = n // 2 if wrap else n - 1
    k_dn = n - 1 - k_up if wrap else n - 1

    def perm(step, direction):
        pairs = []
        for i in range(axis_size):
            p = (i // stride) % n
            q = (p + direction) % n if wrap else p + direction
            origin = p - direction * (step - 1)
            if not wrap and not (0 <= q < n and 0 <= origin < n):
                continue
            pairs.append((i, i + (q - p) * stride))
        return pairs

    ups, dns = [], []
    up = dn = block
    for k in range(1, max(k_up, k_dn) + 1):
        if k <= k_up:
            up = lax.ppermute(up, axis, perm(k, 1))
            ups.append(up)
        if k <= k_dn:
            dn = lax.ppermute(dn, axis, perm(k, -1))
            dns.append(dn)
    stacked = jnp.stack([block] + ups + dns)
    j = jnp.arange(n)
    if wrap:
        d = (pos - j) % n
        sel = jnp.where(d == 0, 0, jnp.where(d <= k_up, d, k_up + n - d))
    else:
        d = pos - j
        sel = jnp.where(d == 0, 0, jnp.where(d > 0, d, k_up - d))
    return jnp.take(stacked, sel, axis=0)


def ring_blocks(block, axis):
    n = lax.axis_size(axis)
    right = [(i, (i + 1) % n) for i in range(n)]
    left = [(d, s) for s, d in right]
    got = [(0, block)]
    up = dn = block
    for k in range(1, n // 2 + 1):
        up = lax.ppermute(up, axis, right)
        got.append((k, up))
        if k < n - n // 2:
            dn = lax.ppermute(dn, axis, left)
            got.append((-k, dn))
    return got


def mirrored_pieces(traces, shot_count, recv_count):
    block_rows = traces.shape[2]
    g = traces.shape[3] // block_rows
    me_shot = lax.axis_index(SHOT)
    pieces = []
    for a in range(g):
        got = []
        for h in range(g):
            perm = [
                (s * recv_count + r, (g * r + h) * recv_count + s // g)
                for s in range(a, shot_count, g)
                for r in range(recv_count)
            ]
            part = traces[:, :, :, h * block_rows:(h + 1) * block_rows]
            got.append(lax.ppermute(part, SHOT + RECV, perm))
        pieces.append(jnp.stack(got)[me_shot % g])
    return jnp.concatenate(pieces, axis=2)


def per_device(traces):
    recv_count = lax.axis_size(RECV)
    shot_count = lax.axis_size(SHOT)
    mirrored = mirrored_pieces(traces, shot_count, recv_count)
    summed = traces.astype(jnp.float32) + jnp.swapaxes(mirrored, 2, 3).astype(jnp.float32)
    averaged = (summed * 0.5).astype(jnp.bfloat16)
    freqs, _, block_rows, col_width = averaged.shape
    rows = stream_gather(averaged, "z_hi", True)
    rows = lax.all_gather(rows, "x", axis=1)
    rows = lax.all_gather(rows, "core", axis=2)
    y_n = lax.axis_size("y")
    z_n = lax.axis_size("z_lo")
    row_panel = jnp.transpose(rows, (3, 4, 5, 0, 1, 2, 6)).reshape(freqs, 2, block_rows, z_n, y_n, block_rows)
    me_y = lax.axis_index("y")
    z_cols = jnp.moveaxis(stream_gather(averaged, "z_lo", False), 0, 2)
    blocks = ring_blocks(z_cols, "y")
    real, imag = row_panel[:, 0], row_panel[:, 1]
    paired = jnp.stack((jnp.stack((real, -imag), axis=1), jnp.stack((imag, real), axis=1)), axis=1)
    paired = jnp.transpose(paired, (5, 0, 1, 2, 4, 3, 6))
    product = None
    for offset, col_block in blocks:
        row_block = lax.dynamic_index_in_dim(paired, (me_y - offset) % y_n, axis=0, keepdims=False)
        part = jnp.einsum("fgczik,fczkj->fgij", row_block, col_block, preferred_element_type=jnp.float32)
        product = part if product is None else product + part
    scale_factor = jnp.float32(float(NS) ** (-0.5))
    return product * scale_factor


def solution(mesh):
    fine = Mesh(mesh.devices.reshape(4, 8, 2, 4, 2), SHOT + RECV)
    placed = P(None, None, SHOT, RECV)
    return jax.shard_map(
        per_device,
        mesh=fine,
        in_specs=(placed,),
        out_specs=placed,
        check_vma=False,
    )
```
